256 devices in a mesh: space: 16 (over x, z_hi), snap: 16 (over y, z_lo, core).
Axes of the slice: x: 4, y: 4, z: 8 (z_hi: 4, z_lo: 2; z = z_hi * 2 + z_lo), core: 2. Of those that a mesh axis runs over, the one named last changes fastest.
Arguments:
- velocity: bfloat16 [256, 3, 128, 32, 128], P('snap', None, 'space'), may hold values from -40 to 40
- phase_bins: int32 [256], replicated, may hold values from 0 to 23, as said below
- tile_owner: int32 [16], replicated, may hold values from 0 to 15, each once
Outputs:
- gram_tiles: float32 [16, 16, 256], P('space', None, 'snap')
The draws below stay inside these ranges and needn't reach their ends.
Inputs may be any that keep to these rules, and one draw needn't show every extreme that they name: `phase_bins`: every bin holds at least one snapshot. `tile_owner`: each tile has exactly one owner.
All inputs are finite; a program needn't handle non-finite values.
Results may differ from the reference program's by a relative error of at most 0.0003.
Values may be sent and summed in bfloat16 or wider, within the bound.
No kernel may reach another device: no remote copies, remote signals or barrier semaphores. Data moves between devices by JAX's collectives and lax.ppermute only.
A program may use at most 128 MiB of HBM per device.

```python
import math
import jax
import jax.numpy as jnp
from jax import lax

NY = 32
NZ = 128
NB = 24
S = 256
NX = 128
NT = 16
NVOX = 524288


event_rate = 1.0 / 1024.0


event_low = 8.0


event_ratio = 38.0 / 8.0


def common_bins(key):
    key_draw = jax.random.fold_in(key, 101)
    key_cover = jax.random.fold_in(key, 202)
    raw_value = jax.random.randint(key_draw, (S,), 0, NB * NB, dtype=jnp.int32)
    levels = jnp.arange(1, NB, dtype=jnp.int32)
    bins_drawn = jnp.sum((levels[None, :] * levels[None, :] <= raw_value[:, None]).astype(jnp.int32), axis=1)
    chosen = jax.random.permutation(key_cover, S)[:NB]
    return bins_drawn.at[chosen].set(jnp.arange(NB, dtype=jnp.int32))


def draw_phase_bins(key, part):
    return common_bins(key)


def draw_velocity(key, part):
    bins_all = common_bins(key)
    key_phase = jax.random.fold_in(key, 303)
    key_amp = jax.random.fold_in(key, 404)
    key_mode = jax.random.fold_in(key, 505)
    key_frame = jax.random.fold_in(key, 606)
    phase_shapes = 0.8 * jax.random.normal(key_phase, (2, 3, NX, NY, NZ), jnp.float32)
    mode_shapes = jax.random.normal(key_mode, (4, 3, NX, NY, NZ), jnp.float32)
    amplitude = 0.3 * jax.random.normal(key_amp, (S, 4), jnp.float32)

    def one_frame(index):
        angle = 2.0 * math.pi * bins_all[index].astype(jnp.float32) / NB
        frame_key = jax.random.fold_in(key_frame, index)
        key_noise = jax.random.fold_in(frame_key, 1)
        key_spot = jax.random.fold_in(frame_key, 2)
        key_sign = jax.random.fold_in(frame_key, 3)
        shape = (3, NX, NY, NZ)
        noise_part = 0.5 * jax.random.normal(key_noise, shape, jnp.float32)
        spot = jax.random.uniform(key_spot, shape, jnp.float32)
        sign_draw = jax.random.normal(key_sign, shape, jnp.float32)
        fraction = jnp.minimum(spot / event_rate, 1.0)
        magnitude = event_low * jnp.exp(fraction * math.log(event_ratio))
        events = jnp.where(spot < event_rate, jnp.where(sign_draw < 0.0, -magnitude, magnitude), 0.0)
        row = amplitude[index]
        coherent = row[0] * mode_shapes[0] + row[1] * mode_shapes[1]
        coherent = coherent + row[2] * mode_shapes[2] + row[3] * mode_shapes[3]
        locked = jnp.cos(angle) * phase_shapes[0] + jnp.sin(angle) * phase_shapes[1]
        field_value = locked + coherent + noise_part + events
        return jnp.clip(field_value, -40.0, 40.0).astype(jnp.bfloat16)
    return lax.map(one_frame, jnp.arange(S, dtype=jnp.int32))


def setup_inputs(seed: int = 0) -> dict:
    key_of = jax.random.split(jax.random.key(seed), 4)
    velocity = draw_velocity(jax.random.fold_in(key_of[3], 71), 0)
    phase_bins = draw_phase_bins(jax.random.fold_in(key_of[3], 71), 0)
    tile_owner = jax.random.permutation(key_of[2], NT).astype(jnp.int32)
    return {"velocity": velocity, "phase_bins": phase_bins, "tile_owner": tile_owner}


def widen(field_in, direction):
    widths = [(0, 0)] * field_in.ndim
    widths[direction] = (2, 2)
    return jnp.pad(field_in, widths)


def derivative(padded_field, direction):
    length = padded_field.shape[direction] - 4

    def window_at(offset):
        return lax.slice_in_dim(padded_field, offset, offset + length, axis=direction)

    return (8.0 * (window_at(3) - window_at(1)) - (window_at(4) - window_at(0))) / 12.0


def curl_field(u_field, v_field, w_field, v_wide, w_wide, first):
    second = first + 1
    third = first + 2
    omega_x = derivative(widen(w_field, second), second) - derivative(widen(v_field, third), third)
    omega_y = derivative(widen(u_field, third), third) - derivative(w_wide, first)
    omega_z = derivative(v_wide, first) - derivative(widen(u_field, second), second)
    return jnp.stack([omega_x, omega_y, omega_z], axis=first)


def reference(velocity, phase_bins, tile_owner):
    def one_snapshot(frame):
        frame_float = frame.astype(jnp.float32)
        v_wide = widen(frame_float[1], 0)
        w_wide = widen(frame_float[2], 0)
        return curl_field(frame_float[0], frame_float[1], frame_float[2], v_wide, w_wide, 0).astype(jnp.bfloat16)

    vortex = lax.map(one_snapshot, velocity)
    planes = jnp.transpose(vortex, (2, 0, 1, 3, 4)).reshape(NX, S, 3 * NY * NZ)
    onehot = (phase_bins[None, :] == jnp.arange(NB, dtype=jnp.int32)[:, None]).astype(jnp.bfloat16)
    bin_counts = jnp.sum(onehot.astype(jnp.float32), axis=1)

    def accumulate(running, voxel_plane):
        bin_sums = jnp.dot(onehot, voxel_plane, preferred_element_type=jnp.float32)
        bin_means = bin_sums / bin_counts[:, None]
        fluctuation = (voxel_plane.astype(jnp.float32) - jnp.take(bin_means, phase_bins, axis=0)).astype(jnp.bfloat16)
        product = lax.dot_general(fluctuation, fluctuation, (((1,), (1,)), ((), ())), preferred_element_type=jnp.float32)
        return running + product, None

    gram_sum, _ = lax.scan(accumulate, jnp.zeros((S, S), jnp.float32), planes)
    gram_sum = gram_sum / NVOX
    blocks = gram_sum.reshape(NT, S // NT, S)
    tile_ids = jnp.arange(NT, dtype=jnp.int32)
    inverse = jnp.sum(tile_ids[None, :] * (tile_owner[None, :] == tile_ids[:, None]).astype(jnp.int32), axis=1)
    return jnp.take(blocks, inverse, axis=0)
```

```python
import jax
import jax.numpy as jnp
from jax import lax
from jax.sharding import PartitionSpec as P

NB = 24


def x_halo(block, width):
    count = lax.axis_size("space")
    forward = [(i, i + 1) for i in range(count - 1)]
    backward = [(target, source) for source, target in forward]
    low = lax.ppermute(block[:, :, block.shape[2] - width :], "space", forward)
    high = lax.ppermute(block[:, :, :width], "space", backward)
    return jnp.concatenate([low, block, high], axis=2)


def stencil(window_at):
    return (8.0 * (window_at(3) - window_at(1)) - (window_at(4) - window_at(0))) / 12.0


def d_padded(field, axis):
    widths = [(0, 0)] * field.ndim
    widths[axis] = (2, 2)
    padded = jnp.pad(field, widths)
    length = field.shape[axis]
    return stencil(lambda o: lax.slice_in_dim(padded, o, o + length, axis=axis))


def d_wide(wide, axis):
    length = wide.shape[axis] - 4
    return stencil(lambda o: lax.slice_in_dim(wide, o, o + length, axis=axis))


def all_to_all_sum(x, axis):
    got = lax.all_to_all(x, axis, split_axis=0, concat_axis=0, tiled=True)
    return jnp.sum(got, axis=0)


def per_device(velocity, phase_bins, tile_owner):
    snaps_dev, _, cells_x, cells_y, cells_z = velocity.shape
    vw_wide = x_halo(velocity[:, 1:3], 2).astype(jnp.float32)
    frame = velocity.astype(jnp.float32)
    u, v, w = frame[:, 0], frame[:, 1], frame[:, 2]
    v_wide, w_wide = vw_wide[:, 0], vw_wide[:, 1]
    omega_x = d_padded(w, 2) - d_padded(v, 3)
    omega_y = d_padded(u, 3) - d_wide(w_wide, 1)
    omega_z = d_wide(v_wide, 1) - d_padded(u, 2)
    vortex = jnp.stack([omega_x, omega_y, omega_z], axis=1).astype(jnp.bfloat16)

    n_snap = lax.axis_size("snap")
    halves = n_snap // cells_x
    rows = cells_y // halves
    parts = vortex.reshape(snaps_dev, 3, cells_x, halves, rows, cells_z)
    parts = jnp.transpose(parts, (2, 3, 0, 1, 4, 5)).reshape(n_snap, snaps_dev, 3, rows, cells_z)
    arranged = lax.all_to_all(parts, "snap", split_axis=0, concat_axis=0, tiled=True)
    total_snaps = n_snap * snaps_dev
    columns = arranged.reshape(total_snaps, 3 * rows, cells_z)

    onehot = (phase_bins[None, :] == jnp.arange(NB, dtype=jnp.int32)[:, None])
    bin_counts = jnp.sum(onehot.astype(jnp.float32), axis=1)
    bin_sums = jnp.einsum(
        "bs,skz->bkz", onehot.astype(jnp.bfloat16), columns, preferred_element_type=jnp.float32
    )
    bin_means = bin_sums / bin_counts[:, None, None]
    selected = jnp.einsum(
        "sb,bkz->skz",
        onehot.T.astype(jnp.float32),
        bin_means,
        precision=lax.Precision.HIGHEST,
        preferred_element_type=jnp.float32,
    )
    fluctuation = (columns.astype(jnp.float32) - selected).astype(jnp.bfloat16)
    voxel_total = lax.axis_size("space") * cells_x * cells_y * cells_z
    partial_gram = (
        jnp.einsum("skz,tkz->st", fluctuation, fluctuation, preferred_element_type=jnp.float32)
        / voxel_total
    )

    row_blocks = partial_gram.reshape(n_snap, total_snaps // n_snap, total_snaps)
    col_sum = all_to_all_sum(row_blocks, "snap")
    tile_count = lax.axis_size("space")
    tile_ids = jnp.arange(tile_count, dtype=jnp.int32)
    inverse = jnp.sum(
        tile_ids[None, :] * (tile_owner[None, :] == tile_ids[:, None]).astype(jnp.int32), axis=1
    )
    tiles = col_sum.reshape(col_sum.shape[0], tile_count, total_snaps // tile_count)
    tiles = jnp.transpose(jnp.take(tiles, inverse, axis=1), (1, 2, 0))
    mine = all_to_all_sum(tiles, "space")
    return mine[None]


def solution(mesh):
    return jax.shard_map(
        per_device,
        mesh=mesh,
        in_specs=(P("snap", None, "space", None, None), P(), P()),
        out_specs=P("space", None, "snap"),
        check_vma=False,
    )
```

```python
import jax
import jax.numpy as jnp
from jax import lax
from jax.sharding import PartitionSpec as P

NB = 24


def x_halo(block, width):
    count = lax.axis_size("space")
    forward = [(i, i + 1) for i in range(count - 1)]
    backward = [(target, source) for source, target in forward]
    low = lax.ppermute(block[:, :, block.shape[2] - width :], "space", forward)
    high = lax.ppermute(block[:, :, :width], "space", backward)
    return jnp.concatenate([low, block, high], axis=2)


def stencil(window_at):
    return (8.0 * (window_at(3) - window_at(1)) - (window_at(4) - window_at(0))) / 12.0


def d_padded(field, axis):
    widths = [(0, 0)] * field.ndim
    widths[axis] = (2, 2)
    padded = jnp.pad(field, widths)
    length = field.shape[axis]
    return stencil(lambda o: lax.slice_in_dim(padded, o, o + length, axis=axis))


def d_wide(wide, axis):
    length = wide.shape[axis] - 4
    return stencil(lambda o: lax.slice_in_dim(wide, o, o + length, axis=axis))


def all_to_all_sum(x, axis):
    got = lax.all_to_all(x, axis, split_axis=0, concat_axis=0, tiled=True)
    return jnp.sum(got, axis=0)


def to_parts(field, n_snap):
    snaps_dev, cells_x, cells_y, cells_z = field.shape
    halves = n_snap // cells_x
    rows = cells_y // halves
    parts = field.reshape(snaps_dev, cells_x, halves, rows, cells_z)
    return jnp.transpose(parts, (1, 2, 0, 3, 4)).reshape(n_snap, snaps_dev, rows, cells_z)


def exchange(parts):
    arranged = lax.all_to_all(parts, "snap", split_axis=0, concat_axis=0, tiled=True)
    count, snaps_dev, comps, rows, cells_z = arranged.shape
    return arranged.reshape(count * snaps_dev, comps * rows, cells_z)


def fluctuation_of(columns, onehot, bin_counts):
    bin_sums = jnp.einsum(
        "bs,skz->bkz", onehot.astype(jnp.bfloat16), columns, preferred_element_type=jnp.float32
    )
    bin_means = bin_sums / bin_counts[:, None, None]
    selected = jnp.einsum(
        "sb,bkz->skz",
        onehot.T.astype(jnp.float32),
        bin_means,
        precision=lax.Precision.HIGHEST,
        preferred_element_type=jnp.float32,
    )
    fluct = (columns.astype(jnp.float32) - selected).astype(jnp.bfloat16)
    return jnp.einsum("skz,tkz->st", fluct, fluct, preferred_element_type=jnp.float32)


def per_device(velocity, phase_bins, tile_owner):
    snaps_dev, _, cells_x, cells_y, cells_z = velocity.shape
    n_snap = lax.axis_size("snap")
    vw_wide = x_halo(velocity[:, 1:3], 2)
    frame = velocity.astype(jnp.float32)
    u, v, w = frame[:, 0], frame[:, 1], frame[:, 2]

    omega_x = (d_padded(w, 2) - d_padded(v, 3)).astype(jnp.bfloat16)
    cols_x = exchange(to_parts(omega_x, n_snap)[:, :, None])

    vw_wide = vw_wide.astype(jnp.float32)
    v_wide, w_wide = vw_wide[:, 0], vw_wide[:, 1]
    omega_y = d_padded(u, 3) - d_wide(w_wide, 1)
    omega_z = d_wide(v_wide, 1) - d_padded(u, 2)
    omega_yz = jnp.stack(
        [to_parts(omega_y.astype(jnp.bfloat16), n_snap), to_parts(omega_z.astype(jnp.bfloat16), n_snap)],
        axis=2,
    )
    cols_yz = exchange(omega_yz)
    total_snaps = cols_x.shape[0]

    onehot = (phase_bins[None, :] == jnp.arange(NB, dtype=jnp.int32)[:, None])
    bin_counts = jnp.sum(onehot.astype(jnp.float32), axis=1)
    voxel_total = lax.axis_size("space") * cells_x * cells_y * cells_z
    partial_gram = (
        fluctuation_of(cols_x, onehot, bin_counts) + fluctuation_of(cols_yz, onehot, bin_counts)
    ) / voxel_total

    row_blocks = partial_gram.reshape(n_snap, total_snaps // n_snap, total_snaps)
    col_sum = all_to_all_sum(row_blocks, "snap")
    tile_count = lax.axis_size("space")
    tile_ids = jnp.arange(tile_count, dtype=jnp.int32)
    inverse = jnp.sum(
        tile_ids[None, :] * (tile_owner[None, :] == tile_ids[:, None]).astype(jnp.int32), axis=1
    )
    tiles = col_sum.reshape(col_sum.shape[0], tile_count, total_snaps // tile_count)
    tiles = jnp.transpose(jnp.take(tiles, inverse, axis=1), (1, 2, 0))
    mine = all_to_all_sum(tiles, "space")
    return mine[None]


def solution(mesh):
    return jax.shard_map(
        per_device,
        mesh=mesh,
        in_specs=(P("snap", None, "space", None, None), P(), P()),
        out_specs=P("space", None, "snap"),
        check_vma=False,
    )
```

```python
import jax
import jax.numpy as jnp
from jax import lax
from jax.sharding import PartitionSpec as P


NB = 24


def x_halo(block, width):
    count = lax.axis_size("space")
    forward = [(i, i + 1) for i in range(count - 1)]
    backward = [(target, source) for source, target in forward]
    low = lax.ppermute(block[:, :, block.shape[2] - width :], "space", forward)
    high = lax.ppermute(block[:, :, :width], "space", backward)
    return jnp.concatenate([low, block, high], axis=2)


def stencil(window_at):
    return (8.0 * (window_at(3) - window_at(1)) - (window_at(4) - window_at(0))) / 12.0


def d_padded(field, axis):
    widths = [(0, 0)] * field.ndim
    widths[axis] = (2, 2)
    padded = jnp.pad(field, widths)
    length = field.shape[axis]
    return stencil(lambda o: lax.slice_in_dim(padded, o, o + length, axis=axis))


def all_to_all_sum(x, axis):
    got = lax.all_to_all(x, axis, split_axis=0, concat_axis=0, tiled=True)
    return jnp.sum(got, axis=0)


def pieces(field, count):
    snaps_dev, cells_z = field.shape[0], field.shape[-1]
    blocks = field.reshape(snaps_dev, count, -1, cells_z)
    return jnp.transpose(blocks, (1, 0, 2, 3))


def exchange(parts):
    arranged = lax.all_to_all(parts, "snap", split_axis=0, concat_axis=0, tiled=True)
    count, snaps_dev, comps, rows, cells_z = arranged.shape
    return arranged.reshape(count * snaps_dev, comps * rows, cells_z)


def fluctuation_of(columns, onehot, bin_counts):
    bin_sums = jnp.einsum(
        "bs,skz->bkz", onehot.astype(jnp.bfloat16), columns, preferred_element_type=jnp.float32
    )
    bin_means = bin_sums / bin_counts[:, None, None]
    selected = jnp.einsum(
        "sb,bkz->skz",
        onehot.T.astype(jnp.float32),
        bin_means,
        precision=lax.Precision.HIGHEST,
        preferred_element_type=jnp.float32,
    )
    fluct = (columns.astype(jnp.float32) - selected).astype(jnp.bfloat16)
    return jnp.einsum("skz,tkz->st", fluct, fluct, preferred_element_type=jnp.float32)


def d_x(field, planes):
    return stencil(lambda o: field[:, planes[0] + o - 2 : planes[-1] + o - 1])


def body(velocity, phase_bins, tile_owner):
    _, _, cells_x, cells_y, cells_z = velocity.shape
    n_snap = lax.axis_size("snap")
    frame = velocity.astype(jnp.float32)
    u, v, w = frame[:, 0], frame[:, 1], frame[:, 2]
    inner = list(range(2, cells_x - 2))

    omega_x = (d_padded(w, 2) - d_padded(v, 3)).astype(jnp.bfloat16)
    u_in = u[:, inner[0] : inner[-1] + 1]
    omega_y_in = (d_padded(u_in, 3) - d_x(w, inner)).astype(jnp.bfloat16)
    omega_z_in = (d_x(v, inner) - d_padded(u_in, 2)).astype(jnp.bfloat16)
    early = jnp.stack(
        [pieces(omega_x, n_snap), pieces(jnp.stack([omega_y_in, omega_z_in], axis=1), n_snap)], axis=2
    )
    cols_a = exchange(early)

    vw_wide = x_halo(velocity[:, 1:3], 2)
    vw_wide = vw_wide.astype(jnp.float32)
    v_wide, w_wide = vw_wide[:, 0], vw_wide[:, 1]
    u_edge = jnp.concatenate([u[:, :2], u[:, cells_x - 2 :]], axis=1)
    dxw = jnp.concatenate([d_x(w_wide, [2, 3]), d_x(w_wide, [cells_x, cells_x + 1])], axis=1)
    dxv = jnp.concatenate([d_x(v_wide, [2, 3]), d_x(v_wide, [cells_x, cells_x + 1])], axis=1)
    omega_y_edge = (d_padded(u_edge, 3) - dxw).astype(jnp.bfloat16)
    omega_z_edge = (dxv - d_padded(u_edge, 2)).astype(jnp.bfloat16)
    late = pieces(jnp.stack([omega_y_edge, omega_z_edge], axis=1), n_snap)[:, :, None]
    cols_b = exchange(late)
    total_snaps = cols_a.shape[0]

    onehot = (phase_bins[None, :] == jnp.arange(NB, dtype=jnp.int32)[:, None])
    bin_counts = jnp.sum(onehot.astype(jnp.float32), axis=1)
    voxel_total = lax.axis_size("space") * cells_x * cells_y * cells_z
    partial_gram = (
        fluctuation_of(cols_a, onehot, bin_counts) + fluctuation_of(cols_b, onehot, bin_counts)
    ) / voxel_total

    row_blocks = partial_gram.reshape(n_snap, total_snaps // n_snap, total_snaps)
    col_sum = all_to_all_sum(row_blocks, "snap")
    tile_count = lax.axis_size("space")
    tile_ids = jnp.arange(tile_count, dtype=jnp.int32)
    inverse = jnp.sum(
        tile_ids[None, :] * (tile_owner[None, :] == tile_ids[:, None]).astype(jnp.int32), axis=1
    )
    tiles = col_sum.reshape(col_sum.shape[0], tile_count, total_snaps // tile_count)
    tiles = jnp.transpose(jnp.take(tiles, inverse, axis=1), (1, 2, 0))
    mine = all_to_all_sum(tiles, "space")
    return mine[None]


def solution(mesh):
    return jax.shard_map(
        body,
        mesh=mesh,
        in_specs=(P("snap", None, "space", None, None), P(), P()),
        out_specs=P("space", None, "snap"),
        check_vma=False,
    )
```

```python
import jax
import jax.numpy as jnp
from jax import lax
from jax.experimental import pallas as pl
from jax.experimental.pallas import tpu as pltpu
from jax.sharding import PartitionSpec as P

NB = 24


def x_halo(block, width):
    count = lax.axis_size("space")
    forward = [(i, i + 1) for i in range(count - 1)]
    backward = [(target, source) for source, target in forward]
    low = lax.ppermute(block[:, :, block.shape[2] - width :], "space", forward)
    high = lax.ppermute(block[:, :, :width], "space", backward)
    return jnp.concatenate([low, block, high], axis=2)


def stencil(window_at):
    return (8.0 * (window_at(3) - window_at(1)) - (window_at(4) - window_at(0))) / 12.0


def d_padded(field, axis):
    widths = [(0, 0)] * field.ndim
    widths[axis] = (2, 2)
    padded = jnp.pad(field, widths)
    length = field.shape[axis]
    return stencil(lambda o: lax.slice_in_dim(padded, o, o + length, axis=axis))


def d_wide(wide, axis):
    length = wide.shape[axis] - 4
    return stencil(lambda o: lax.slice_in_dim(wide, o, o + length, axis=axis))


def shifted(f, offset, axis):
    size = f.shape[axis]
    rolled = pltpu.roll(f, (-offset) % size, axis)
    index = lax.broadcasted_iota(jnp.int32, f.shape, axis) + offset
    return jnp.where((index >= 0) & (index < size), rolled, 0.0)


def d_in(f, axis):
    return stencil(lambda o: shifted(f, o - 2, axis))


def curl_x_kernel(vel_ref, out_ref):
    cells_x, cells_y = vel_ref.shape[2], vel_ref.shape[3]
    rows = out_ref.shape[3]
    for x in range(cells_x):
        v = vel_ref[0, 1, x].astype(jnp.float32)
        w = vel_ref[0, 2, x].astype(jnp.float32)
        omega = (d_in(w, 0) - d_in(v, 1)).astype(out_ref.dtype)
        for h in range(cells_y // rows):
            out_ref[x * (cells_y // rows) + h, 0, 0] = omega[h * rows : (h + 1) * rows]


def curl_yz_kernel(vel_ref, low_ref, high_ref, out_ref):
    cells_x, cells_y = vel_ref.shape[2], vel_ref.shape[3]
    rows = out_ref.shape[3]

    def plane(c, x):
        if x < 0:
            return low_ref[0, c - 1, x + 2].astype(jnp.float32)
        if x >= cells_x:
            return high_ref[0, c - 1, x - cells_x].astype(jnp.float32)
        return vel_ref[0, c, x].astype(jnp.float32)

    for x in range(cells_x):
        u = vel_ref[0, 0, x].astype(jnp.float32)
        dxw = stencil(lambda o: plane(2, x + o - 2))
        dxv = stencil(lambda o: plane(1, x + o - 2))
        omega_y = (d_in(u, 1) - dxw).astype(out_ref.dtype)
        omega_z = (dxv - d_in(u, 0)).astype(out_ref.dtype)
        for h in range(cells_y // rows):
            out_ref[x * (cells_y // rows) + h, 0, 0] = omega_y[h * rows : (h + 1) * rows]
            out_ref[x * (cells_y // rows) + h, 0, 1] = omega_z[h * rows : (h + 1) * rows]


def curl_call(kernel, comps, velocity, halos, n_snap):
    snaps_dev, _, cells_x, cells_y, cells_z = velocity.shape
    rows = cells_y * cells_x // n_snap
    vel_spec = pl.BlockSpec((1,) + velocity.shape[1:], lambda s: (s, 0, 0, 0, 0))
    halo_specs = [pl.BlockSpec((1,) + h.shape[1:], lambda s: (s, 0, 0, 0, 0)) for h in halos]
    return pl.pallas_call(
        kernel,
        grid=(snaps_dev,),
        in_specs=[vel_spec] + halo_specs,
        out_specs=pl.BlockSpec((n_snap, 1, comps, rows, cells_z), lambda s: (0, s, 0, 0, 0)),
        out_shape=jax.ShapeDtypeStruct((n_snap, snaps_dev, comps, rows, cells_z), jnp.bfloat16),
    )(velocity, *halos)


def all_to_all_sum(x, axis):
    got = lax.all_to_all(x, axis, split_axis=0, concat_axis=0, tiled=True)
    return jnp.sum(got, axis=0)


def to_parts(field, n_snap):
    snaps_dev, cells_x, cells_y, cells_z = field.shape
    halves = n_snap // cells_x
    rows = cells_y // halves
    parts = field.reshape(snaps_dev, cells_x, halves, rows, cells_z)
    return jnp.transpose(parts, (1, 2, 0, 3, 4)).reshape(n_snap, snaps_dev, rows, cells_z)


def exchange(parts):
    arranged = lax.all_to_all(parts, "snap", split_axis=0, concat_axis=0, tiled=True)
    count, snaps_dev, comps, rows, cells_z = arranged.shape
    return arranged.reshape(count * snaps_dev, comps * rows, cells_z)


def fluctuation_of(columns, onehot, bin_counts):
    bin_sums = jnp.einsum(
        "bs,skz->bkz", onehot.astype(jnp.bfloat16), columns, preferred_element_type=jnp.float32
    )
    bin_means = bin_sums / bin_counts[:, None, None]
    selected = jnp.einsum(
        "sb,bkz->skz",
        onehot.T.astype(jnp.float32),
        bin_means,
        precision=lax.Precision.HIGHEST,
        preferred_element_type=jnp.float32,
    )
    fluct = (columns.astype(jnp.float32) - selected).astype(jnp.bfloat16)
    return jnp.einsum("skz,tkz->st", fluct, fluct, preferred_element_type=jnp.float32)


def per_device(velocity, phase_bins, tile_owner):
    snaps_dev, _, cells_x, cells_y, cells_z = velocity.shape
    n_snap = lax.axis_size("snap")
    count = lax.axis_size("space")
    forward = [(i, i + 1) for i in range(count - 1)]
    backward = [(target, source) for source, target in forward]
    low = lax.ppermute(velocity[:, 1:3, cells_x - 2 :], "space", forward)
    high = lax.ppermute(velocity[:, 1:3, :2], "space", backward)

    cols_x = exchange(curl_call(curl_x_kernel, 1, velocity, [], n_snap))
    cols_yz = exchange(curl_call(curl_yz_kernel, 2, velocity, [low, high], n_snap))
    total_snaps = cols_x.shape[0]

    onehot = (phase_bins[None, :] == jnp.arange(NB, dtype=jnp.int32)[:, None])
    bin_counts = jnp.sum(onehot.astype(jnp.float32), axis=1)
    voxel_total = lax.axis_size("space") * cells_x * cells_y * cells_z
    partial_gram = (
        fluctuation_of(cols_x, onehot, bin_counts) + fluctuation_of(cols_yz, onehot, bin_counts)
    ) / voxel_total

    row_blocks = partial_gram.reshape(n_snap, total_snaps // n_snap, total_snaps)
    col_sum = all_to_all_sum(row_blocks, "snap")
    tile_count = lax.axis_size("space")
    tile_ids = jnp.arange(tile_count, dtype=jnp.int32)
    inverse = jnp.sum(
        tile_ids[None, :] * (tile_owner[None, :] == tile_ids[:, None]).astype(jnp.int32), axis=1
    )
    tiles = col_sum.reshape(col_sum.shape[0], tile_count, total_snaps // tile_count)
    tiles = jnp.transpose(jnp.take(tiles, inverse, axis=1), (1, 2, 0))
    mine = all_to_all_sum(tiles, "space")
    return mine[None]


def solution(mesh):
    return jax.shard_map(
        per_device,
        mesh=mesh,
        in_specs=(P("snap", None, "space", None, None), P(), P()),
        out_specs=P("space", None, "snap"),
        check_vma=False,
    )
```

```python
import jax
import jax.numpy as jnp
from jax import lax
from jax.experimental import pallas as pl
from jax.experimental.pallas import tpu as pltpu
from jax.sharding import PartitionSpec as P


NB = 24


def stencil(window_at):
    return (8.0 * (window_at(3) - window_at(1)) - (window_at(4) - window_at(0))) / 12.0


def shifters(shape):
    masks = {}
    for axis in (0, 1):
        index = lax.broadcasted_iota(jnp.int32, shape, axis)
        for offset in (-2, -1, 1, 2):
            masks[axis, offset] = (index + offset >= 0) & (index + offset < shape[axis])

    def shifted(f, offset, axis):
        rolled = pltpu.roll(f, (-offset) % shape[axis], axis)
        return jnp.where(masks[axis, offset], rolled, 0.0)

    def d_in(f, axis):
        return (8.0 * (shifted(f, 1, axis) - shifted(f, -1, axis)) - (shifted(f, 2, axis) - shifted(f, -2, axis))) / 12.0

    return d_in


def curl_x_kernel(vel_ref, out_ref):
    snaps, _, cells_x, cells_y, _ = vel_ref.shape
    rows = out_ref.shape[3]
    d_in = shifters(vel_ref.shape[3:])
    for s in range(snaps):
        for x in range(cells_x):
            v = vel_ref[s, 1, x].astype(jnp.float32)
            w = vel_ref[s, 2, x].astype(jnp.float32)
            omega = (d_in(w, 0) - d_in(v, 1)).astype(out_ref.dtype)
            for h in range(cells_y // rows):
                out_ref[x * (cells_y // rows) + h, s, 0] = omega[h * rows : (h + 1) * rows]


def curl_yz_kernel(vel_ref, low_ref, high_ref, out_ref):
    snaps, _, cells_x, cells_y, _ = vel_ref.shape
    rows = out_ref.shape[3]
    d_in = shifters(vel_ref.shape[3:])
    for s in range(snaps):
        wide = []
        for c in (1, 2):
            planes = [low_ref[s, c - 1, i] for i in range(2)]
            planes += [vel_ref[s, c, i] for i in range(cells_x)]
            planes += [high_ref[s, c - 1, i] for i in range(2)]
            wide.append([p.astype(jnp.float32) for p in planes])
        v_wide, w_wide = wide
        for x in range(cells_x):
            u = vel_ref[s, 0, x].astype(jnp.float32)
            dxw = stencil(lambda o: w_wide[x + o])
            dxv = stencil(lambda o: v_wide[x + o])
            omega_y = (d_in(u, 1) - dxw).astype(out_ref.dtype)
            omega_z = (dxv - d_in(u, 0)).astype(out_ref.dtype)
            for h in range(cells_y // rows):
                out_ref[x * (cells_y // rows) + h, s, 0] = omega_y[h * rows : (h + 1) * rows]
                out_ref[x * (cells_y // rows) + h, s, 1] = omega_z[h * rows : (h + 1) * rows]


def curl_call(kernel, comps, velocity, halos, n_snap):
    snaps_dev, _, cells_x, cells_y, cells_z = velocity.shape
    rows = cells_y * cells_x // n_snap
    block = 4
    vel_spec = pl.BlockSpec((block,) + velocity.shape[1:], lambda s: (s, 0, 0, 0, 0))
    halo_specs = [pl.BlockSpec((block,) + h.shape[1:], lambda s: (s, 0, 0, 0, 0)) for h in halos]
    return pl.pallas_call(
        kernel,
        grid=(snaps_dev // block,),
        in_specs=[vel_spec] + halo_specs,
        out_specs=pl.BlockSpec((n_snap, block, comps, rows, cells_z), lambda s: (0, s, 0, 0, 0)),
        out_shape=jax.ShapeDtypeStruct((n_snap, snaps_dev, comps, rows, cells_z), jnp.bfloat16),
    )(velocity, *halos)


def all_to_all_sum(x, axis):
    got = lax.all_to_all(x, axis, split_axis=0, concat_axis=0, tiled=True)
    return jnp.sum(got, axis=0)


def exchange(parts):
    arranged = lax.all_to_all(parts, "snap", split_axis=0, concat_axis=0, tiled=True)
    count, snaps_dev, comps, rows, cells_z = arranged.shape
    return arranged.reshape(count * snaps_dev, comps * rows, cells_z)


def fluctuation_of(columns, onehot, bin_counts):
    bin_sums = jnp.einsum(
        "bs,skz->bkz", onehot.astype(jnp.bfloat16), columns, preferred_element_type=jnp.float32
    )
    bin_means = bin_sums / bin_counts[:, None, None]
    selected = jnp.einsum(
        "sb,bkz->skz",
        onehot.T.astype(jnp.float32),
        bin_means,
        precision=lax.Precision.HIGHEST,
        preferred_element_type=jnp.float32,
    )
    fluct = (columns.astype(jnp.float32) - selected).astype(jnp.bfloat16)
    return jnp.einsum("skz,tkz->st", fluct, fluct, preferred_element_type=jnp.float32)


def body(velocity, phase_bins, tile_owner):
    _, _, cells_x, cells_y, cells_z = velocity.shape
    n_snap = lax.axis_size("snap")
    count = lax.axis_size("space")
    forward = [(i, i + 1) for i in range(count - 1)]
    backward = [(target, source) for source, target in forward]
    low = lax.ppermute(velocity[:, 1:3, cells_x - 2 :], "space", forward)
    high = lax.ppermute(velocity[:, 1:3, :2], "space", backward)

    parts_x = curl_call(curl_x_kernel, 1, velocity, [], n_snap)
    cols_x = exchange(parts_x)
    cols_yz = exchange(curl_call(curl_yz_kernel, 2, velocity, [low, high], n_snap))
    total_snaps = cols_x.shape[0]

    onehot = (phase_bins[None, :] == jnp.arange(NB, dtype=jnp.int32)[:, None])
    bin_counts = jnp.sum(onehot.astype(jnp.float32), axis=1)
    voxel_total = lax.axis_size("space") * cells_x * cells_y * cells_z
    partial_gram = (
        fluctuation_of(cols_x, onehot, bin_counts) + fluctuation_of(cols_yz, onehot, bin_counts)
    ) / voxel_total

    row_blocks = partial_gram.reshape(n_snap, total_snaps // n_snap, total_snaps)
    col_sum = all_to_all_sum(row_blocks, "snap")
    tile_count = lax.axis_size("space")
    tile_ids = jnp.arange(tile_count, dtype=jnp.int32)
    inverse = jnp.sum(
        tile_ids[None, :] * (tile_owner[None, :] == tile_ids[:, None]).astype(jnp.int32), axis=1
    )
    tiles = col_sum.reshape(col_sum.shape[0], tile_count, total_snaps // tile_count)
    tiles = jnp.transpose(jnp.take(tiles, inverse, axis=1), (1, 2, 0))
    mine = all_to_all_sum(tiles, "space")
    return mine[None]


def solution(mesh):
    return jax.shard_map(
        body,
        mesh=mesh,
        in_specs=(P("snap", None, "space", None, None), P(), P()),
        out_specs=P("space", None, "snap"),
        check_vma=False,
    )
```

```python
import jax
import jax.numpy as jnp
from jax import lax
from jax.experimental import pallas as pl
from jax.experimental.pallas import tpu as pltpu
from jax.sharding import PartitionSpec as P


NB = 24


def stencil(window_at):
    return (8.0 * (window_at(3) - window_at(1)) - (window_at(4) - window_at(0))) / 12.0


def shifters(shape):
    masks = {}
    for axis in (0, 1):
        index = lax.broadcasted_iota(jnp.int32, shape, axis)
        for offset in (-2, -1, 1, 2):
            masks[axis, offset] = (index + offset >= 0) & (index + offset < shape[axis])

    def shifted(f, offset, axis):
        rolled = pltpu.roll(f, (-offset) % shape[axis], axis)
        return jnp.where(masks[axis, offset], rolled, 0.0)

    def d_in(f, axis):
        return (8.0 * (shifted(f, 1, axis) - shifted(f, -1, axis)) - (shifted(f, 2, axis) - shifted(f, -2, axis))) / 12.0

    return d_in


def curl_early_kernel(vel_ref, out_ref):
    snaps, _, cells_x, cells_y, _ = vel_ref.shape
    rows = out_ref.shape[3]
    halves = cells_y // rows
    inner = cells_x - 4
    d_in = shifters(vel_ref.shape[3:])
    for s in range(snaps):
        planes = [[vel_ref[s, c, i].astype(jnp.float32) for i in range(cells_x)] for c in range(3)]
        u, v, w = planes
        for x in range(cells_x):
            omega = (d_in(w[x], 0) - d_in(v[x], 1)).astype(out_ref.dtype)
            for h in range(halves):
                out_ref[x * halves + h, s, 0] = omega[h * rows : (h + 1) * rows]
            if 2 <= x < cells_x - 2:
                dxw = stencil(lambda o: w[x + o - 2])
                dxv = stencil(lambda o: v[x + o - 2])
                omega_y = (d_in(u[x], 1) - dxw).astype(out_ref.dtype)
                omega_z = (dxv - d_in(u[x], 0)).astype(out_ref.dtype)
                for h in range(halves):
                    out_ref[(x - 2) * halves + h, s, 1] = omega_y[h * rows : (h + 1) * rows]
                    out_ref[(inner + x - 2) * halves + h, s, 1] = omega_z[h * rows : (h + 1) * rows]


def curl_edge_kernel(vel_ref, low_ref, high_ref, out_ref):
    snaps, _, cells_x, cells_y, _ = vel_ref.shape
    rows = out_ref.shape[3]
    halves = cells_y // rows
    d_in = shifters(vel_ref.shape[3:])
    edges = [0, 1, cells_x - 2, cells_x - 1]
    for s in range(snaps):
        wide = []
        for c in (1, 2):
            planes = [low_ref[s, c - 1, i] for i in range(2)]
            planes += [vel_ref[s, c, i] for i in range(cells_x)]
            planes += [high_ref[s, c - 1, i] for i in range(2)]
            wide.append([p.astype(jnp.float32) for p in planes])
        v_wide, w_wide = wide
        for e, x in enumerate(edges):
            u = vel_ref[s, 0, x].astype(jnp.float32)
            dxw = stencil(lambda o: w_wide[x + o])
            dxv = stencil(lambda o: v_wide[x + o])
            omega_y = (d_in(u, 1) - dxw).astype(out_ref.dtype)
            omega_z = (dxv - d_in(u, 0)).astype(out_ref.dtype)
            for h in range(halves):
                out_ref[e * halves + h, s, 0] = omega_y[h * rows : (h + 1) * rows]
                out_ref[(len(edges) + e) * halves + h, s, 0] = omega_z[h * rows : (h + 1) * rows]


def curl_call(kernel, comps, velocity, halos, n_snap):
    snaps_dev, _, cells_x, cells_y, cells_z = velocity.shape
    rows = cells_y * cells_x // n_snap
    block = 4
    vel_spec = pl.BlockSpec((block,) + velocity.shape[1:], lambda s: (s, 0, 0, 0, 0))
    halo_specs = [pl.BlockSpec((block,) + h.shape[1:], lambda s: (s, 0, 0, 0, 0)) for h in halos]
    return pl.pallas_call(
        kernel,
        grid=(snaps_dev // block,),
        in_specs=[vel_spec] + halo_specs,
        out_specs=pl.BlockSpec((n_snap, block, comps, rows, cells_z), lambda s: (0, s, 0, 0, 0)),
        out_shape=jax.ShapeDtypeStruct((n_snap, snaps_dev, comps, rows, cells_z), jnp.bfloat16),
    )(velocity, *halos)


def all_to_all_sum(x, axis):
    got = lax.all_to_all(x, axis, split_axis=0, concat_axis=0, tiled=True)
    return jnp.sum(got, axis=0)


def exchange(parts):
    arranged = lax.all_to_all(parts, "snap", split_axis=0, concat_axis=0, tiled=True)
    count, snaps_dev, comps, rows, cells_z = arranged.shape
    return arranged.reshape(count * snaps_dev, comps * rows, cells_z)


def fluctuation_of(columns, onehot, bin_counts):
    bin_sums = jnp.einsum(
        "bs,skz->bkz", onehot.astype(jnp.bfloat16), columns, preferred_element_type=jnp.float32
    )
    bin_means = bin_sums / bin_counts[:, None, None]
    selected = jnp.einsum(
        "sb,bkz->skz",
        onehot.T.astype(jnp.float32),
        bin_means,
        precision=lax.Precision.HIGHEST,
        preferred_element_type=jnp.float32,
    )
    fluct = (columns.astype(jnp.float32) - selected).astype(jnp.bfloat16)
    return jnp.einsum("skz,tkz->st", fluct, fluct, preferred_element_type=jnp.float32)


def body(velocity, phase_bins, tile_owner):
    _, _, cells_x, cells_y, cells_z = velocity.shape
    n_snap = lax.axis_size("snap")
    count = lax.axis_size("space")
    forward = [(i, i + 1) for i in range(count - 1)]
    backward = [(target, source) for source, target in forward]
    low = lax.ppermute(velocity[:, 1:3, cells_x - 2 :], "space", forward)
    high = lax.ppermute(velocity[:, 1:3, :2], "space", backward)

    parts_x = curl_call(curl_early_kernel, 2, velocity, [], n_snap)
    cols_x = exchange(parts_x)
    low, high, cols_x = lax.optimization_barrier((low, high, cols_x))
    cols_yz = exchange(curl_call(curl_edge_kernel, 1, velocity, [low, high], n_snap))
    total_snaps = cols_x.shape[0]

    onehot = (phase_bins[None, :] == jnp.arange(NB, dtype=jnp.int32)[:, None])
    bin_counts = jnp.sum(onehot.astype(jnp.float32), axis=1)
    voxel_total = lax.axis_size("space") * cells_x * cells_y * cells_z
    partial_gram = (
        fluctuation_of(cols_x, onehot, bin_counts) + fluctuation_of(cols_yz, onehot, bin_counts)
    ) / voxel_total

    row_blocks = partial_gram.reshape(n_snap, total_snaps // n_snap, total_snaps)
    col_sum = all_to_all_sum(row_blocks, "snap")
    tile_count = lax.axis_size("space")
    tile_ids = jnp.arange(tile_count, dtype=jnp.int32)
    inverse = jnp.sum(
        tile_ids[None, :] * (tile_owner[None, :] == tile_ids[:, None]).astype(jnp.int32), axis=1
    )
    tiles = col_sum.reshape(col_sum.shape[0], tile_count, total_snaps // tile_count)
    tiles = jnp.transpose(jnp.take(tiles, inverse, axis=1), (1, 2, 0))
    mine = all_to_all_sum(tiles, "space")
    return mine[None]


def solution(mesh):
    return jax.shard_map(
        body,
        mesh=mesh,
        in_specs=(P("snap", None, "space", None, None), P(), P()),
        out_specs=P("space", None, "snap"),
        check_vma=False,
    )
```

```python
import jax
import jax.numpy as jnp
from jax import lax
from jax.experimental import pallas as pl
from jax.experimental.pallas import tpu as pltpu
from jax.sharding import PartitionSpec as P


NB = 24


def stencil(window_at):
    return (8.0 * (window_at(3) - window_at(1)) - (window_at(4) - window_at(0))) / 12.0


def shifters(shape):
    masks = {}
    for axis in (0, 1):
        index = lax.broadcasted_iota(jnp.int32, shape, axis)
        for offset in (-2, -1, 1, 2):
            masks[axis, offset] = (index + offset >= 0) & (index + offset < shape[axis])

    def shifted(f, offset, axis):
        rolled = pltpu.roll(f, (-offset) % shape[axis], axis)
        return jnp.where(masks[axis, offset], rolled, 0.0)

    def d_in(f, axis):
        return (8.0 * (shifted(f, 1, axis) - shifted(f, -1, axis)) - (shifted(f, 2, axis) - shifted(f, -2, axis))) / 12.0

    return d_in


def curl_early_kernel(vel_ref, out_ref):
    snaps, _, cells_x, cells_y, _ = vel_ref.shape
    rows = out_ref.shape[3]
    halves = cells_y // rows
    inner = cells_x - 4
    d_in = shifters(vel_ref.shape[3:])
    for s in range(snaps):
        planes = [[vel_ref[s, c, i].astype(jnp.float32) for i in range(cells_x)] for c in range(3)]
        u, v, w = planes
        for x in range(cells_x):
            omega = (d_in(w[x], 0) - d_in(v[x], 1)).astype(out_ref.dtype)
            for h in range(halves):
                out_ref[x * halves + h, s, 0] = omega[h * rows : (h + 1) * rows]
            if 2 <= x < cells_x - 2:
                dxw = stencil(lambda o: w[x + o - 2])
                dxv = stencil(lambda o: v[x + o - 2])
                omega_y = (d_in(u[x], 1) - dxw).astype(out_ref.dtype)
                omega_z = (dxv - d_in(u[x], 0)).astype(out_ref.dtype)
                for h in range(halves):
                    out_ref[(x - 2) * halves + h, s, 1] = omega_y[h * rows : (h + 1) * rows]
                    out_ref[(inner + x - 2) * halves + h, s, 1] = omega_z[h * rows : (h + 1) * rows]


def curl_edge_kernel(vel_ref, low_ref, high_ref, _, out_ref):
    snaps, _, cells_x, cells_y, _ = vel_ref.shape
    rows = out_ref.shape[3]
    halves = cells_y // rows
    d_in = shifters(vel_ref.shape[3:])
    edges = [0, 1, cells_x - 2, cells_x - 1]
    for s in range(snaps):
        wide = []
        for c in (1, 2):
            planes = [low_ref[s, c - 1, i] for i in range(2)]
            planes += [vel_ref[s, c, i] for i in range(cells_x)]
            planes += [high_ref[s, c - 1, i] for i in range(2)]
            wide.append([p.astype(jnp.float32) for p in planes])
        v_wide, w_wide = wide
        for e, x in enumerate(edges):
            u = vel_ref[s, 0, x].astype(jnp.float32)
            dxw = stencil(lambda o: w_wide[x + o])
            dxv = stencil(lambda o: v_wide[x + o])
            omega_y = (d_in(u, 1) - dxw).astype(out_ref.dtype)
            omega_z = (dxv - d_in(u, 0)).astype(out_ref.dtype)
            for h in range(halves):
                out_ref[e * halves + h, s, 0] = omega_y[h * rows : (h + 1) * rows]
                out_ref[(len(edges) + e) * halves + h, s, 0] = omega_z[h * rows : (h + 1) * rows]


def curl_call(kernel, comps, velocity, halos, n_snap, slot=0, into=None):
    snaps_dev, _, cells_x, cells_y, cells_z = velocity.shape
    rows = cells_y * cells_x // n_snap
    block = 8
    vel_spec = pl.BlockSpec((block,) + velocity.shape[1:], lambda s: (s, 0, 0, 0, 0))
    halo_specs = [pl.BlockSpec((block,) + h.shape[1:], lambda s: (s, 0, 0, 0, 0)) for h in halos]
    operands = [velocity, *halos]
    in_specs = [vel_spec] + halo_specs
    aliases = {}
    if into is not None:
        operands.append(into)
        in_specs.append(pl.BlockSpec(memory_space=pl.ANY))
        aliases = {len(operands) - 1: 0}
    return pl.pallas_call(
        kernel,
        grid=(snaps_dev // block,),
        in_specs=in_specs,
        out_specs=pl.BlockSpec((n_snap, block, comps, rows, cells_z), lambda s: (0, s, slot, 0, 0)),
        out_shape=jax.ShapeDtypeStruct((n_snap, snaps_dev, 3, rows, cells_z), jnp.bfloat16),
        input_output_aliases=aliases,
    )(*operands)


def all_to_all_sum(x, axis):
    got = lax.all_to_all(x, axis, split_axis=0, concat_axis=0, tiled=True)
    return jnp.sum(got, axis=0)


def exchange(parts):
    arranged = lax.all_to_all(parts, "snap", split_axis=0, concat_axis=0, tiled=True)
    count, snaps_dev, comps, rows, cells_z = arranged.shape
    return arranged.reshape(count * snaps_dev, comps * rows, cells_z)


def fluctuation_of(columns, onehot, bin_counts):
    bin_sums = jnp.einsum(
        "bs,skz->bkz", onehot.astype(jnp.bfloat16), columns, preferred_element_type=jnp.float32
    )
    bin_means = bin_sums / bin_counts[:, None, None]
    selected = jnp.einsum(
        "sb,bkz->skz",
        onehot.T.astype(jnp.float32),
        bin_means,
        precision=lax.Precision.HIGHEST,
        preferred_element_type=jnp.float32,
    )
    fluct = (columns.astype(jnp.float32) - selected).astype(jnp.bfloat16)
    return jnp.einsum("skz,tkz->st", fluct, fluct, preferred_element_type=jnp.float32)


def body(velocity, phase_bins, tile_owner):
    _, _, cells_x, cells_y, cells_z = velocity.shape
    n_snap = lax.axis_size("snap")
    count = lax.axis_size("space")
    forward = [(i, i + 1) for i in range(count - 1)]
    backward = [(target, source) for source, target in forward]
    low = lax.ppermute(velocity[:, 1:3, cells_x - 2 :], "space", forward)
    high = lax.ppermute(velocity[:, 1:3, :2], "space", backward)

    parts = curl_call(curl_early_kernel, 2, velocity, [], n_snap)
    parts = curl_call(curl_edge_kernel, 1, velocity, [low, high], n_snap, slot=2, into=parts)
    columns = exchange(parts)
    total_snaps = columns.shape[0]

    onehot = (phase_bins[None, :] == jnp.arange(NB, dtype=jnp.int32)[:, None])
    bin_counts = jnp.sum(onehot.astype(jnp.float32), axis=1)
    voxel_total = lax.axis_size("space") * cells_x * cells_y * cells_z
    partial_gram = (
        fluctuation_of(columns, onehot, bin_counts)
    ) / voxel_total

    row_blocks = partial_gram.reshape(n_snap, total_snaps // n_snap, total_snaps)
    col_sum = all_to_all_sum(row_blocks, "snap")
    tile_count = lax.axis_size("space")
    tile_ids = jnp.arange(tile_count, dtype=jnp.int32)
    inverse = jnp.sum(
        tile_ids[None, :] * (tile_owner[None, :] == tile_ids[:, None]).astype(jnp.int32), axis=1
    )
    tiles = col_sum.reshape(col_sum.shape[0], tile_count, total_snaps // tile_count)
    tiles = jnp.transpose(jnp.take(tiles, inverse, axis=1), (1, 2, 0))
    mine = all_to_all_sum(tiles, "space")
    return mine[None]


def solution(mesh):
    return jax.shard_map(
        body,
        mesh=mesh,
        in_specs=(P("snap", None, "space", None, None), P(), P()),
        out_specs=P("space", None, "snap"),
        check_vma=False,
    )
```

```python
import jax
import jax.numpy as jnp
from jax import lax
from jax.experimental import pallas as pl
from jax.experimental.pallas import tpu as pltpu
from jax.sharding import PartitionSpec as P


NB = 24


def stencil(window_at):
    return (8.0 * (window_at(3) - window_at(1)) - (window_at(4) - window_at(0))) / 12.0


def shifters(shape):
    masks = {}
    for axis in (0, 1):
        index = lax.broadcasted_iota(jnp.int32, shape, axis)
        for offset in (-2, -1, 1, 2):
            masks[axis, offset] = (index + offset >= 0) & (index + offset < shape[axis])

    def shifted(f, offset, axis):
        rolled = pltpu.roll(f, (-offset) % shape[axis], axis)
        return jnp.where(masks[axis, offset], rolled, 0.0)

    def d_in(f, axis):
        return (8.0 * (shifted(f, 1, axis) - shifted(f, -1, axis)) - (shifted(f, 2, axis) - shifted(f, -2, axis))) / 12.0

    return d_in


def curl_x_kernel(vel_ref, out_ref):
    snaps, _, cells_x, cells_y, _ = vel_ref.shape
    rows = out_ref.shape[3]
    d_in = shifters(vel_ref.shape[3:])
    for s in range(snaps):
        for x in range(cells_x):
            v = vel_ref[s, 1, x].astype(jnp.float32)
            w = vel_ref[s, 2, x].astype(jnp.float32)
            omega = (d_in(w, 0) - d_in(v, 1)).astype(out_ref.dtype)
            for h in range(cells_y // rows):
                out_ref[x * (cells_y // rows) + h, s, 0] = omega[h * rows : (h + 1) * rows]


def curl_yz_kernel(vel_ref, low_ref, high_ref, out_ref):
    snaps, _, cells_x, cells_y, _ = vel_ref.shape
    rows = out_ref.shape[3]
    d_in = shifters(vel_ref.shape[3:])
    for s in range(snaps):
        wide = []
        for c in (1, 2):
            planes = [low_ref[s, c - 1, i] for i in range(2)]
            planes += [vel_ref[s, c, i] for i in range(cells_x)]
            planes += [high_ref[s, c - 1, i] for i in range(2)]
            wide.append([p.astype(jnp.float32) for p in planes])
        v_wide, w_wide = wide
        for x in range(cells_x):
            u = vel_ref[s, 0, x].astype(jnp.float32)
            dxw = stencil(lambda o: w_wide[x + o])
            dxv = stencil(lambda o: v_wide[x + o])
            omega_y = (d_in(u, 1) - dxw).astype(out_ref.dtype)
            omega_z = (dxv - d_in(u, 0)).astype(out_ref.dtype)
            for h in range(cells_y // rows):
                out_ref[x * (cells_y // rows) + h, s, 0] = omega_y[h * rows : (h + 1) * rows]
                out_ref[x * (cells_y // rows) + h, s, 1] = omega_z[h * rows : (h + 1) * rows]


def curl_call(kernel, comps, velocity, halos, n_snap):
    snaps_dev, _, cells_x, cells_y, cells_z = velocity.shape
    rows = cells_y * cells_x // n_snap
    block = 8
    vel_spec = pl.BlockSpec((block,) + velocity.shape[1:], lambda s: (s, 0, 0, 0, 0))
    halo_specs = [pl.BlockSpec((block,) + h.shape[1:], lambda s: (s, 0, 0, 0, 0)) for h in halos]
    return pl.pallas_call(
        kernel,
        grid=(snaps_dev // block,),
        in_specs=[vel_spec] + halo_specs,
        out_specs=pl.BlockSpec((n_snap, block, comps, rows, cells_z), lambda s: (0, s, 0, 0, 0)),
        out_shape=jax.ShapeDtypeStruct((n_snap, snaps_dev, comps, rows, cells_z), jnp.bfloat16),
    )(velocity, *halos)


def all_to_all_sum(x, axis):
    got = lax.all_to_all(x, axis, split_axis=0, concat_axis=0, tiled=True)
    return jnp.sum(got, axis=0)


def exchange(parts):
    arranged = lax.all_to_all(parts, "snap", split_axis=0, concat_axis=0, tiled=True)
    count, snaps_dev, comps, rows, cells_z = arranged.shape
    return arranged.reshape(count * snaps_dev, comps * rows, cells_z)


def fluctuation_of(columns, onehot, bin_counts):
    bin_sums = jnp.einsum(
        "bs,skz->bkz", onehot.astype(jnp.bfloat16), columns, preferred_element_type=jnp.float32
    )
    bin_means = bin_sums / bin_counts[:, None, None]
    selected = jnp.einsum(
        "sb,bkz->skz",
        onehot.T.astype(jnp.float32),
        bin_means,
        precision=lax.Precision.HIGHEST,
        preferred_element_type=jnp.float32,
    )
    fluct = (columns.astype(jnp.float32) - selected).astype(jnp.bfloat16)
    fluct = fluct.reshape(fluct.shape[0], -1)
    return jnp.einsum("sk,tk->st", fluct, fluct, preferred_element_type=jnp.float32)


def body(velocity, phase_bins, tile_owner):
    _, _, cells_x, cells_y, cells_z = velocity.shape
    n_snap = lax.axis_size("snap")
    count = lax.axis_size("space")
    forward = [(i, i + 1) for i in range(count - 1)]
    backward = [(target, source) for source, target in forward]
    low = lax.ppermute(velocity[:, 1:3, cells_x - 2 :], "space", forward)
    high = lax.ppermute(velocity[:, 1:3, :2], "space", backward)

    parts_x = curl_call(curl_x_kernel, 1, velocity, [], n_snap)
    cols_x = exchange(parts_x)
    cols_yz = exchange(curl_call(curl_yz_kernel, 2, velocity, [low, high], n_snap))
    total_snaps = cols_x.shape[0]

    onehot = (phase_bins[None, :] == jnp.arange(NB, dtype=jnp.int32)[:, None])
    bin_counts = jnp.sum(onehot.astype(jnp.float32), axis=1)
    voxel_total = lax.axis_size("space") * cells_x * cells_y * cells_z
    partial_gram = (
        fluctuation_of(cols_x, onehot, bin_counts) + fluctuation_of(cols_yz, onehot, bin_counts)
    ) / voxel_total

    row_blocks = partial_gram.reshape(n_snap, total_snaps // n_snap, total_snaps)
    col_sum = all_to_all_sum(row_blocks, "snap")
    tile_count = lax.axis_size("space")
    tile_ids = jnp.arange(tile_count, dtype=jnp.int32)
    inverse = jnp.sum(
        tile_ids[None, :] * (tile_owner[None, :] == tile_ids[:, None]).astype(jnp.int32), axis=1
    )
    tiles = col_sum.reshape(col_sum.shape[0], tile_count, total_snaps // tile_count)
    tiles = jnp.transpose(jnp.take(tiles, inverse, axis=1), (1, 2, 0))
    mine = all_to_all_sum(tiles, "space")
    return mine[None]


def solution(mesh):
    return jax.shard_map(
        body,
        mesh=mesh,
        in_specs=(P("snap", None, "space", None, None), P(), P()),
        out_specs=P("space", None, "snap"),
        check_vma=False,
    )
```

```python
import jax
import jax.numpy as jnp
from jax import lax
from jax.experimental import pallas as pl
from jax.experimental.pallas import tpu as pltpu
from jax.sharding import PartitionSpec as P


NB = 24


def stencil(window_at):
    return (8.0 * (window_at(3) - window_at(1)) - (window_at(4) - window_at(0))) / 12.0


def shifters(shape):
    masks = {}
    for axis in (0, 1):
        index = lax.broadcasted_iota(jnp.int32, shape, axis)
        for offset in (-2, -1, 1, 2):
            masks[axis, offset] = (index + offset >= 0) & (index + offset < shape[axis])

    def shifted(f, offset, axis):
        rolled = pltpu.roll(f, (-offset) % shape[axis], axis)
        return jnp.where(masks[axis, offset], rolled, 0.0)

    def d_in(f, axis):
        return (8.0 * (shifted(f, 1, axis) - shifted(f, -1, axis)) - (shifted(f, 2, axis) - shifted(f, -2, axis))) / 12.0

    return d_in


def curl_x_kernel(vel_ref, out_ref):
    snaps, _, cells_x, cells_y, _ = vel_ref.shape
    rows = out_ref.shape[3]
    d_in = shifters(vel_ref.shape[3:])
    for s in range(snaps):
        for x in range(cells_x):
            v = vel_ref[s, 1, x].astype(jnp.float32)
            w = vel_ref[s, 2, x].astype(jnp.float32)
            omega = (d_in(w, 0) - d_in(v, 1)).astype(out_ref.dtype)
            for h in range(cells_y // rows):
                out_ref[x * (cells_y // rows) + h, s, 0] = omega[h * rows : (h + 1) * rows]


def curl_yz_kernel(vel_ref, low_ref, high_ref, out_ref):
    snaps, _, cells_x, cells_y, _ = vel_ref.shape
    rows = out_ref.shape[3]
    d_in = shifters(vel_ref.shape[3:])
    for s in range(snaps):
        wide = []
        for c in (1, 2):
            planes = [low_ref[s, c - 1, i] for i in range(2)]
            planes += [vel_ref[s, c, i] for i in range(cells_x)]
            planes += [high_ref[s, c - 1, i] for i in range(2)]
            wide.append([p.astype(jnp.float32) for p in planes])
        v_wide, w_wide = wide
        for x in range(cells_x):
            u = vel_ref[s, 0, x].astype(jnp.float32)
            dxw = stencil(lambda o: w_wide[x + o])
            dxv = stencil(lambda o: v_wide[x + o])
            omega_y = (d_in(u, 1) - dxw).astype(out_ref.dtype)
            omega_z = (dxv - d_in(u, 0)).astype(out_ref.dtype)
            for h in range(cells_y // rows):
                out_ref[x * (cells_y // rows) + h, s, 0] = omega_y[h * rows : (h + 1) * rows]
                out_ref[x * (cells_y // rows) + h, s, 1] = omega_z[h * rows : (h + 1) * rows]


def curl_call(kernel, comps, velocity, halos, n_snap):
    snaps_dev, _, cells_x, cells_y, cells_z = velocity.shape
    rows = cells_y * cells_x // n_snap
    block = 8
    vel_spec = pl.BlockSpec((block,) + velocity.shape[1:], lambda s: (s, 0, 0, 0, 0))
    halo_specs = [pl.BlockSpec((block,) + h.shape[1:], lambda s: (s, 0, 0, 0, 0)) for h in halos]
    return pl.pallas_call(
        kernel,
        grid=(snaps_dev // block,),
        in_specs=[vel_spec] + halo_specs,
        out_specs=pl.BlockSpec((n_snap, block, comps, rows, cells_z), lambda s: (0, s, 0, 0, 0)),
        out_shape=jax.ShapeDtypeStruct((n_snap, snaps_dev, comps, rows, cells_z), jnp.bfloat16),
    )(velocity, *halos)


def all_to_all_sum(x, axis):
    got = lax.all_to_all(x, axis, split_axis=0, concat_axis=0, tiled=True)
    return jnp.sum(got, axis=0)


def exchange(parts):
    arranged = lax.all_to_all(parts, "snap", split_axis=0, concat_axis=0, tiled=True)
    count, snaps_dev, comps, rows, cells_z = arranged.shape
    return arranged.reshape(count * snaps_dev, comps * rows, cells_z)


def fluctuation_of(columns, onehot, bin_counts):
    bin_sums = jnp.einsum(
        "bs,skz->bkz", onehot.astype(jnp.bfloat16), columns, preferred_element_type=jnp.float32
    )
    bin_means = bin_sums / bin_counts[:, None, None]
    selected = jnp.einsum(
        "sb,bkz->skz",
        onehot.T.astype(jnp.float32),
        bin_means,
        precision=lax.Precision.HIGHEST,
        preferred_element_type=jnp.float32,
    )
    fluct = (columns.astype(jnp.float32) - selected).astype(jnp.bfloat16)
    return jnp.einsum("skz,tkz->st", fluct, fluct, preferred_element_type=jnp.float32)


def body(velocity, phase_bins, tile_owner):
    _, _, cells_x, cells_y, cells_z = velocity.shape
    n_snap = lax.axis_size("snap")
    count = lax.axis_size("space")
    forward = [(i, i + 1) for i in range(count - 1)]
    backward = [(target, source) for source, target in forward]
    low = lax.ppermute(velocity[:, 1:3, cells_x - 2 :], "space", forward)
    high = lax.ppermute(velocity[:, 1:3, :2], "space", backward)

    parts_x = curl_call(curl_x_kernel, 1, velocity, [], n_snap)
    cols_x = exchange(parts_x)
    cols_yz = exchange(curl_call(curl_yz_kernel, 2, velocity, [low, high], n_snap))
    total_snaps = cols_x.shape[0]

    onehot = (phase_bins[None, :] == jnp.arange(NB, dtype=jnp.int32)[:, None])
    bin_counts = jnp.sum(onehot.astype(jnp.float32), axis=1)
    voxel_total = lax.axis_size("space") * cells_x * cells_y * cells_z
    partial_gram = (
        fluctuation_of(cols_x, onehot, bin_counts) + fluctuation_of(cols_yz, onehot, bin_counts)
    ) / voxel_total

    row_blocks = partial_gram.reshape(n_snap, total_snaps // n_snap, total_snaps)
    col_sum = all_to_all_sum(row_blocks, "snap")
    tile_count = lax.axis_size("space")
    tile_ids = jnp.arange(tile_count, dtype=jnp.int32)
    owned = (tile_owner[None, :] == tile_ids[:, None]).astype(jnp.float32)
    tiles = col_sum.reshape(col_sum.shape[0], tile_count, total_snaps // tile_count)
    tiles = jnp.einsum(
        "kt,atr->kra", owned, tiles, precision=lax.Precision.HIGHEST, preferred_element_type=jnp.float32
    )
    mine = all_to_all_sum(tiles, "space")
    return mine[None]


def solution(mesh):
    return jax.shard_map(
        body,
        mesh=mesh,
        in_specs=(P("snap", None, "space", None, None), P(), P()),
        out_specs=P("space", None, "snap"),
        check_vma=False,
    )
```

```python
import jax
import jax.numpy as jnp
from jax import lax
from jax.experimental import pallas as pl
from jax.experimental.pallas import tpu as pltpu
from jax.sharding import PartitionSpec as P


NB = 24


def stencil(window_at):
    return (8.0 * (window_at(3) - window_at(1)) - (window_at(4) - window_at(0))) / 12.0


def shifters(shape):
    masks = {}
    for axis in (0, 1):
        index = lax.broadcasted_iota(jnp.int32, shape, axis)
        for offset in (-2, -1, 1, 2):
            masks[axis, offset] = (index + offset >= 0) & (index + offset < shape[axis])

    def shifted(f, offset, axis):
        rolled = pltpu.roll(f, (-offset) % shape[axis], axis)
        return jnp.where(masks[axis, offset], rolled, 0.0)

    def d_in(f, axis):
        return (8.0 * (shifted(f, 1, axis) - shifted(f, -1, axis)) - (shifted(f, 2, axis) - shifted(f, -2, axis))) / 12.0

    return d_in


def curl_x_kernel(vel_ref, out_ref):
    snaps, _, cells_x, cells_y, _ = vel_ref.shape
    rows = out_ref.shape[3]
    d_in = shifters(vel_ref.shape[3:])
    for s in range(snaps):
        for x in range(cells_x):
            v = vel_ref[s, 1, x].astype(jnp.float32)
            w = vel_ref[s, 2, x].astype(jnp.float32)
            omega = (d_in(w, 0) - d_in(v, 1)).astype(out_ref.dtype)
            for h in range(cells_y // rows):
                out_ref[x * (cells_y // rows) + h, s, 0] = omega[h * rows : (h + 1) * rows]


def curl_yz_kernel(vel_ref, low_ref, high_ref, out_ref):
    snaps, _, cells_x, cells_y, _ = vel_ref.shape
    rows = out_ref.shape[3]
    d_in = shifters(vel_ref.shape[3:])
    for s in range(snaps):
        wide = []
        for c in (1, 2):
            planes = [low_ref[s, c - 1, i] for i in range(2)]
            planes += [vel_ref[s, c, i] for i in range(cells_x)]
            planes += [high_ref[s, c - 1, i] for i in range(2)]
            wide.append([p.astype(jnp.float32) for p in planes])
        v_wide, w_wide = wide
        for x in range(cells_x):
            u = vel_ref[s, 0, x].astype(jnp.float32)
            dxw = stencil(lambda o: w_wide[x + o])
            dxv = stencil(lambda o: v_wide[x + o])
            omega_y = (d_in(u, 1) - dxw).astype(out_ref.dtype)
            omega_z = (dxv - d_in(u, 0)).astype(out_ref.dtype)
            for h in range(cells_y // rows):
                out_ref[x * (cells_y // rows) + h, s, 0] = omega_y[h * rows : (h + 1) * rows]
                out_ref[x * (cells_y // rows) + h, s, 1] = omega_z[h * rows : (h + 1) * rows]


def curl_call(kernel, comps, velocity, halos, n_snap):
    snaps_dev, _, cells_x, cells_y, cells_z = velocity.shape
    rows = cells_y * cells_x // n_snap
    block = 8
    vel_spec = pl.BlockSpec((block,) + velocity.shape[1:], lambda s: (s, 0, 0, 0, 0))
    halo_specs = [pl.BlockSpec((block,) + h.shape[1:], lambda s: (s, 0, 0, 0, 0)) for h in halos]
    return pl.pallas_call(
        kernel,
        grid=(snaps_dev // block,),
        in_specs=[vel_spec] + halo_specs,
        out_specs=pl.BlockSpec((n_snap, block, comps, rows, cells_z), lambda s: (0, s, 0, 0, 0)),
        out_shape=jax.ShapeDtypeStruct((n_snap, snaps_dev, comps, rows, cells_z), jnp.bfloat16),
    )(velocity, *halos)


def all_to_all_sum(x, axis):
    got = lax.all_to_all(x, axis, split_axis=0, concat_axis=0, tiled=True)
    return jnp.sum(got, axis=0)


def exchange(parts):
    arranged = lax.all_to_all(parts, "snap", split_axis=0, concat_axis=0, tiled=True)
    count, snaps_dev, comps, rows, cells_z = arranged.shape
    return arranged.reshape(count * snaps_dev, comps * rows, cells_z)


def fluctuation_of(columns, onehot, bin_counts):
    bin_sums = jnp.einsum(
        "bs,skz->bkz", onehot.astype(jnp.bfloat16), columns, preferred_element_type=jnp.float32
    )
    bin_means = bin_sums / bin_counts[:, None, None]
    selected = jnp.einsum(
        "sb,bkz->skz",
        onehot.T.astype(jnp.float32),
        bin_means,
        precision=lax.Precision.HIGHEST,
        preferred_element_type=jnp.float32,
    )
    fluct = (columns.astype(jnp.float32) - selected).astype(jnp.bfloat16)
    return jnp.einsum("skz,tkz->st", fluct, fluct, preferred_element_type=jnp.float32)


def body(velocity, phase_bins, tile_owner):
    _, _, cells_x, cells_y, cells_z = velocity.shape
    n_snap = lax.axis_size("snap")
    count = lax.axis_size("space")
    forward = [(i, i + 1) for i in range(count - 1)]
    backward = [(target, source) for source, target in forward]
    low = lax.ppermute(velocity[:, 1:3, cells_x - 2 :], "space", forward)
    high = lax.ppermute(velocity[:, 1:3, :2], "space", backward)

    parts_x = curl_call(curl_x_kernel, 1, velocity, [], n_snap)
    cols_x = exchange(parts_x)
    cols_yz = exchange(curl_call(curl_yz_kernel, 2, velocity, [low, high], n_snap))
    total_snaps = cols_x.shape[0]

    onehot = (phase_bins[None, :] == jnp.arange(NB, dtype=jnp.int32)[:, None])
    bin_counts = jnp.sum(onehot.astype(jnp.float32), axis=1)
    voxel_total = lax.axis_size("space") * cells_x * cells_y * cells_z
    partial_gram = (
        fluctuation_of(cols_x, onehot, bin_counts) + fluctuation_of(cols_yz, onehot, bin_counts)
    ) / voxel_total

    row_blocks = partial_gram.reshape(n_snap, total_snaps // n_snap, total_snaps)
    col_sum = all_to_all_sum(row_blocks, "snap")
    tile_count = lax.axis_size("space")
    tile_ids = jnp.arange(tile_count, dtype=jnp.int32)
    owned = (tile_owner[None, :] == tile_ids[:, None]).astype(jnp.float32)
    tiles = col_sum.reshape(col_sum.shape[0], tile_count, total_snaps // tile_count)
    tiles = jnp.einsum(
        "kt,atr->kra", owned, tiles, precision=lax.Precision.HIGHEST, preferred_element_type=jnp.float32
    )
    lanes = 128
    mine = all_to_all_sum(tiles.reshape(tile_count, -1, lanes), "space")
    return mine.reshape(1, total_snaps // tile_count, -1)


def solution(mesh):
    return jax.shard_map(
        body,
        mesh=mesh,
        in_specs=(P("snap", None, "space", None, None), P(), P()),
        out_specs=P("space", None, "snap"),
        check_vma=False,
    )
```

```python
import jax
import jax.numpy as jnp
from jax import lax
from jax.experimental import pallas as pl
from jax.experimental.pallas import tpu as pltpu
from jax.sharding import PartitionSpec as P


NB = 24


def stencil(window_at):
    return (8.0 * (window_at(3) - window_at(1)) - (window_at(4) - window_at(0))) / 12.0


def shifters(shape):
    masks = {}
    for axis in (0, 1):
        index = lax.broadcasted_iota(jnp.int32, shape, axis)
        for offset in (-2, -1, 1, 2):
            masks[axis, offset] = (index + offset >= 0) & (index + offset < shape[axis])

    def shifted(f, offset, axis):
        rolled = pltpu.roll(f, (-offset) % shape[axis], axis)
        return jnp.where(masks[axis, offset], rolled, 0.0)

    def d_in(f, axis):
        return (8.0 * (shifted(f, 1, axis) - shifted(f, -1, axis)) - (shifted(f, 2, axis) - shifted(f, -2, axis))) / 12.0

    return d_in


def curl_x_kernel(vel_ref, out_ref):
    snaps, _, cells_x, cells_y, _ = vel_ref.shape
    rows = out_ref.shape[3]
    d_in = shifters(vel_ref.shape[3:])
    for s in range(snaps):
        for x in range(cells_x):
            v = vel_ref[s, 1, x].astype(jnp.float32)
            w = vel_ref[s, 2, x].astype(jnp.float32)
            omega = (d_in(w, 0) - d_in(v, 1)).astype(out_ref.dtype)
            for h in range(cells_y // rows):
                out_ref[x * (cells_y // rows) + h, s, 0] = omega[h * rows : (h + 1) * rows]


def curl_yz_kernel(vel_ref, low_ref, high_ref, out_ref):
    snaps, _, cells_x, cells_y, _ = vel_ref.shape
    rows = out_ref.shape[3]
    d_in = shifters(vel_ref.shape[3:])
    for s in range(snaps):
        wide = []
        for c in (1, 2):
            planes = [low_ref[s, c - 1, i] for i in range(2)]
            planes += [vel_ref[s, c, i] for i in range(cells_x)]
            planes += [high_ref[s, c - 1, i] for i in range(2)]
            wide.append([p.astype(jnp.float32) for p in planes])
        v_wide, w_wide = wide
        for x in range(cells_x):
            u = vel_ref[s, 0, x].astype(jnp.float32)
            dxw = stencil(lambda o: w_wide[x + o])
            dxv = stencil(lambda o: v_wide[x + o])
            omega_y = (d_in(u, 1) - dxw).astype(out_ref.dtype)
            omega_z = (dxv - d_in(u, 0)).astype(out_ref.dtype)
            for h in range(cells_y // rows):
                out_ref[x * (cells_y // rows) + h, s, 0] = omega_y[h * rows : (h + 1) * rows]
                out_ref[x * (cells_y // rows) + h, s, 1] = omega_z[h * rows : (h + 1) * rows]


def curl_call(kernel, comps, velocity, halos, n_snap):
    snaps_dev, _, cells_x, cells_y, cells_z = velocity.shape
    rows = cells_y * cells_x // n_snap
    block = 8
    vel_spec = pl.BlockSpec((block,) + velocity.shape[1:], lambda s: (s, 0, 0, 0, 0))
    halo_specs = [pl.BlockSpec((block,) + h.shape[1:], lambda s: (s, 0, 0, 0, 0)) for h in halos]
    return pl.pallas_call(
        kernel,
        grid=(snaps_dev // block,),
        in_specs=[vel_spec] + halo_specs,
        out_specs=pl.BlockSpec((n_snap, block, comps, rows, cells_z), lambda s: (0, s, 0, 0, 0)),
        out_shape=jax.ShapeDtypeStruct((n_snap, snaps_dev, comps, rows, cells_z), jnp.bfloat16),
    )(velocity, *halos)


def all_to_all_sum(x, axis):
    got = lax.all_to_all(x, axis, split_axis=0, concat_axis=0, tiled=True)
    return jnp.sum(got, axis=0)


def exchange(parts):
    arranged = lax.all_to_all(parts, "snap", split_axis=0, concat_axis=0, tiled=True)
    count, snaps_dev, comps, rows, cells_z = arranged.shape
    return arranged.reshape(count * snaps_dev, comps * rows, cells_z)


def fluctuation_of(columns, onehot, bin_counts):
    bin_sums = jnp.einsum(
        "bs,skz->bkz", onehot.astype(jnp.bfloat16), columns, preferred_element_type=jnp.float32
    )
    bin_means = bin_sums / bin_counts[:, None, None]
    high = lax.reduce_precision(bin_means, exponent_bits=8, mantissa_bits=7)
    rest = bin_means - high
    middle = lax.reduce_precision(rest, exponent_bits=8, mantissa_bits=7)
    split = jnp.concatenate([high, middle, rest - middle], axis=0).astype(jnp.bfloat16)
    selected = jnp.einsum(
        "sb,bkz->skz",
        jnp.tile(onehot.T.astype(jnp.bfloat16), (1, 3)),
        split,
        preferred_element_type=jnp.float32,
    )
    fluct = (columns.astype(jnp.float32) - selected).astype(jnp.bfloat16)
    return jnp.einsum("skz,tkz->st", fluct, fluct, preferred_element_type=jnp.float32)


def body(velocity, phase_bins, tile_owner):
    _, _, cells_x, cells_y, cells_z = velocity.shape
    n_snap = lax.axis_size("snap")
    count = lax.axis_size("space")
    forward = [(i, i + 1) for i in range(count - 1)]
    backward = [(target, source) for source, target in forward]
    low = lax.ppermute(velocity[:, 1:3, cells_x - 2 :], "space", forward)
    high = lax.ppermute(velocity[:, 1:3, :2], "space", backward)

    parts_x = curl_call(curl_x_kernel, 1, velocity, [], n_snap)
    cols_x = exchange(parts_x)
    cols_yz = exchange(curl_call(curl_yz_kernel, 2, velocity, [low, high], n_snap))
    total_snaps = cols_x.shape[0]

    onehot = (phase_bins[None, :] == jnp.arange(NB, dtype=jnp.int32)[:, None])
    bin_counts = jnp.sum(onehot.astype(jnp.float32), axis=1)
    voxel_total = lax.axis_size("space") * cells_x * cells_y * cells_z
    partial_gram = (
        fluctuation_of(cols_x, onehot, bin_counts) + fluctuation_of(cols_yz, onehot, bin_counts)
    ) / voxel_total

    row_blocks = partial_gram.reshape(n_snap, total_snaps // n_snap, total_snaps)
    col_sum = all_to_all_sum(row_blocks, "snap")
    tile_count = lax.axis_size("space")
    tile_ids = jnp.arange(tile_count, dtype=jnp.int32)
    owned = (tile_owner[None, :] == tile_ids[:, None]).astype(jnp.float32)
    tiles = col_sum.reshape(col_sum.shape[0], tile_count, total_snaps // tile_count)
    tiles = jnp.einsum(
        "kt,atr->kra", owned, tiles, precision=lax.Precision.HIGHEST, preferred_element_type=jnp.float32
    )
    lanes = 128
    cols = tiles.shape[2]
    padded = jnp.pad(tiles, ((0, 0), (0, 0), (0, lanes - cols)))
    mine = all_to_all_sum(padded, "space")
    return mine[None, :, :cols]


def solution(mesh):
    return jax.shard_map(
        body,
        mesh=mesh,
        in_specs=(P("snap", None, "space", None, None), P(), P()),
        out_specs=P("space", None, "snap"),
        check_vma=False,
    )
```

```python
import jax
import jax.numpy as jnp
from jax import lax
from jax.experimental import pallas as pl
from jax.experimental.pallas import tpu as pltpu
from jax.sharding import PartitionSpec as P


NB = 24


def stencil(window_at):
    return (8.0 * (window_at(3) - window_at(1)) - (window_at(4) - window_at(0))) / 12.0


def shifters(shape):
    masks = {}
    for axis in (0, 1):
        index = lax.broadcasted_iota(jnp.int32, shape, axis)
        for offset in (-2, -1, 1, 2):
            masks[axis, offset] = (index + offset >= 0) & (index + offset < shape[axis])

    def shifted(f, offset, axis):
        rolled = pltpu.roll(f, (-offset) % shape[axis], axis)
        return jnp.where(masks[axis, offset], rolled, 0.0)

    def d_in(f, axis):
        return (8.0 * (shifted(f, 1, axis) - shifted(f, -1, axis)) - (shifted(f, 2, axis) - shifted(f, -2, axis))) / 12.0

    return d_in


def curl_x_kernel(vel_ref, out_ref):
    snaps, _, cells_x, cells_y, _ = vel_ref.shape
    rows = out_ref.shape[3]
    d_in = shifters(vel_ref.shape[3:])
    for s in range(snaps):
        for x in range(cells_x):
            v = vel_ref[s, 1, x].astype(jnp.float32)
            w = vel_ref[s, 2, x].astype(jnp.float32)
            omega = (d_in(w, 0) - d_in(v, 1)).astype(out_ref.dtype)
            for h in range(cells_y // rows):
                out_ref[x * (cells_y // rows) + h, s, 0] = omega[h * rows : (h + 1) * rows]


def curl_yz_kernel(vel_ref, low_ref, high_ref, out_ref):
    snaps, _, cells_x, cells_y, _ = vel_ref.shape
    rows = out_ref.shape[3]
    d_in = shifters(vel_ref.shape[3:])
    for s in range(snaps):
        wide = []
        for c in (1, 2):
            planes = [low_ref[s, c - 1, i] for i in range(2)]
            planes += [vel_ref[s, c, i] for i in range(cells_x)]
            planes += [high_ref[s, c - 1, i] for i in range(2)]
            wide.append([p.astype(jnp.float32) for p in planes])
        v_wide, w_wide = wide
        for x in range(cells_x):
            u = vel_ref[s, 0, x].astype(jnp.float32)
            dxw = stencil(lambda o: w_wide[x + o])
            dxv = stencil(lambda o: v_wide[x + o])
            omega_y = (d_in(u, 1) - dxw).astype(out_ref.dtype)
            omega_z = (dxv - d_in(u, 0)).astype(out_ref.dtype)
            for h in range(cells_y // rows):
                out_ref[x * (cells_y // rows) + h, s, 0] = omega_y[h * rows : (h + 1) * rows]
                out_ref[x * (cells_y // rows) + h, s, 1] = omega_z[h * rows : (h + 1) * rows]


def curl_call(kernel, comps, velocity, halos, n_snap):
    snaps_dev, _, cells_x, cells_y, cells_z = velocity.shape
    rows = cells_y * cells_x // n_snap
    block = 8
    vel_spec = pl.BlockSpec((block,) + velocity.shape[1:], lambda s: (s, 0, 0, 0, 0))
    halo_specs = [pl.BlockSpec((block,) + h.shape[1:], lambda s: (s, 0, 0, 0, 0)) for h in halos]
    return pl.pallas_call(
        kernel,
        grid=(snaps_dev // block,),
        in_specs=[vel_spec] + halo_specs,
        out_specs=pl.BlockSpec((n_snap, block, comps, rows, cells_z), lambda s: (0, s, 0, 0, 0)),
        out_shape=jax.ShapeDtypeStruct((n_snap, snaps_dev, comps, rows, cells_z), jnp.bfloat16),
    )(velocity, *halos)


def all_to_all_sum(x, axis):
    got = lax.all_to_all(x, axis, split_axis=0, concat_axis=0, tiled=True)
    return jnp.sum(got, axis=0)


def exchange(parts):
    arranged = lax.all_to_all(parts, "snap", split_axis=0, concat_axis=0, tiled=True)
    count, snaps_dev, comps, rows, cells_z = arranged.shape
    return arranged.reshape(count * snaps_dev, comps * rows, cells_z)


def fluctuation_of(columns, onehot, bin_counts):
    bin_sums = jnp.einsum(
        "bs,skz->bkz", onehot.astype(jnp.bfloat16), columns, preferred_element_type=jnp.float32
    )
    bin_means = bin_sums / bin_counts[:, None, None]
    high = lax.reduce_precision(bin_means, exponent_bits=8, mantissa_bits=7)
    rest = bin_means - high
    middle = lax.reduce_precision(rest, exponent_bits=8, mantissa_bits=7)
    split = jnp.concatenate([high, middle, rest - middle], axis=0).astype(jnp.bfloat16)
    selected = jnp.einsum(
        "sb,bkz->skz",
        jnp.tile(onehot.T.astype(jnp.bfloat16), (1, 3)),
        split,
        preferred_element_type=jnp.float32,
    )
    fluct = (columns.astype(jnp.float32) - selected).astype(jnp.bfloat16)
    return jnp.einsum("skz,tkz->st", fluct, fluct, preferred_element_type=jnp.float32)


def body(velocity, phase_bins, tile_owner):
    _, _, cells_x, cells_y, cells_z = velocity.shape
    n_snap = lax.axis_size("snap")
    count = lax.axis_size("space")
    forward = [(i, i + 1) for i in range(count - 1)]
    backward = [(target, source) for source, target in forward]
    low = lax.ppermute(velocity[:, 1:3, cells_x - 2 :], "space", forward)
    high = lax.ppermute(velocity[:, 1:3, :2], "space", backward)

    parts_x = curl_call(curl_x_kernel, 1, velocity, [], n_snap)
    cols_x = exchange(parts_x)
    cols_yz = exchange(curl_call(curl_yz_kernel, 2, velocity, [low, high], n_snap))
    total_snaps = cols_x.shape[0]

    onehot = (phase_bins[None, :] == jnp.arange(NB, dtype=jnp.int32)[:, None])
    bin_counts = jnp.sum(onehot.astype(jnp.float32), axis=1)
    voxel_total = lax.axis_size("space") * cells_x * cells_y * cells_z
    partial_gram = (
        fluctuation_of(cols_x, onehot, bin_counts) + fluctuation_of(cols_yz, onehot, bin_counts)
    ) / voxel_total

    row_blocks = partial_gram.reshape(n_snap, total_snaps // n_snap, total_snaps)
    col_sum = all_to_all_sum(row_blocks, "snap")
    tile_count = lax.axis_size("space")
    tile_ids = jnp.arange(tile_count, dtype=jnp.int32)
    owned = (tile_owner[None, :] == tile_ids[:, None]).astype(jnp.float32)
    tiles = col_sum.reshape(col_sum.shape[0], tile_count, total_snaps // tile_count)
    high = lax.reduce_precision(tiles, exponent_bits=8, mantissa_bits=7)
    rest = tiles - high
    middle = lax.reduce_precision(rest, exponent_bits=8, mantissa_bits=7)
    split = jnp.concatenate([high, middle, rest - middle], axis=1).astype(jnp.bfloat16)
    tiles = jnp.einsum(
        "kt,atr->kra", jnp.tile(owned.astype(jnp.bfloat16), (1, 3)), split, preferred_element_type=jnp.float32
    )
    lanes = 128
    mine = all_to_all_sum(tiles.reshape(tile_count, -1, lanes), "space")
    return mine.reshape(1, total_snaps // tile_count, -1)


def solution(mesh):
    return jax.shard_map(
        body,
        mesh=mesh,
        in_specs=(P("snap", None, "space", None, None), P(), P()),
        out_specs=P("space", None, "snap"),
        check_vma=False,
    )
```

```python
import jax
import jax.numpy as jnp
from jax import lax
from jax.experimental import pallas as pl
from jax.experimental.pallas import tpu as pltpu
from jax.sharding import PartitionSpec as P


NB = 24


def stencil(window_at):
    return (8.0 * (window_at(3) - window_at(1)) - (window_at(4) - window_at(0))) / 12.0


def shifters(shape):
    masks = {}
    for axis in (0, 1):
        index = lax.broadcasted_iota(jnp.int32, shape, axis)
        for offset in (-2, -1, 1, 2):
            masks[axis, offset] = (index + offset >= 0) & (index + offset < shape[axis])

    def shifted(f, offset, axis):
        rolled = pltpu.roll(f, (-offset) % shape[axis], axis)
        return jnp.where(masks[axis, offset], rolled, 0.0)

    def d_in(f, axis):
        return (8.0 * (shifted(f, 1, axis) - shifted(f, -1, axis)) - (shifted(f, 2, axis) - shifted(f, -2, axis))) / 12.0

    return d_in


def curl_x_kernel(vel_ref, out_ref):
    snaps, _, cells_x, cells_y, _ = vel_ref.shape
    rows = out_ref.shape[3]
    d_in = shifters(vel_ref.shape[3:])
    for s in range(snaps):
        for x in range(cells_x):
            v = vel_ref[s, 1, x].astype(jnp.float32)
            w = vel_ref[s, 2, x].astype(jnp.float32)
            omega = (d_in(w, 0) - d_in(v, 1)).astype(out_ref.dtype)
            for h in range(cells_y // rows):
                out_ref[x * (cells_y // rows) + h, s, 0] = omega[h * rows : (h + 1) * rows]


def curl_yz_kernel(vel_ref, low_ref, high_ref, out_ref):
    snaps, _, cells_x, cells_y, _ = vel_ref.shape
    rows = out_ref.shape[3]
    d_in = shifters(vel_ref.shape[3:])
    for s in range(snaps):
        wide = []
        for c in (1, 2):
            planes = [low_ref[s, c - 1, i] for i in range(2)]
            planes += [vel_ref[s, c, i] for i in range(cells_x)]
            planes += [high_ref[s, c - 1, i] for i in range(2)]
            wide.append([p.astype(jnp.float32) for p in planes])
        v_wide, w_wide = wide
        for x in range(cells_x):
            u = vel_ref[s, 0, x].astype(jnp.float32)
            dxw = stencil(lambda o: w_wide[x + o])
            dxv = stencil(lambda o: v_wide[x + o])
            omega_y = (d_in(u, 1) - dxw).astype(out_ref.dtype)
            omega_z = (dxv - d_in(u, 0)).astype(out_ref.dtype)
            for h in range(cells_y // rows):
                out_ref[x * (cells_y // rows) + h, s, 0] = omega_y[h * rows : (h + 1) * rows]
                out_ref[x * (cells_y // rows) + h, s, 1] = omega_z[h * rows : (h + 1) * rows]


def curl_call(kernel, comps, velocity, halos, n_snap):
    snaps_dev, _, cells_x, cells_y, cells_z = velocity.shape
    rows = cells_y * cells_x // n_snap
    block = 8
    vel_spec = pl.BlockSpec((block,) + velocity.shape[1:], lambda s: (s, 0, 0, 0, 0))
    halo_specs = [pl.BlockSpec((block,) + h.shape[1:], lambda s: (s, 0, 0, 0, 0)) for h in halos]
    return pl.pallas_call(
        kernel,
        grid=(snaps_dev // block,),
        in_specs=[vel_spec] + halo_specs,
        out_specs=pl.BlockSpec((n_snap, block, comps, rows, cells_z), lambda s: (0, s, 0, 0, 0)),
        out_shape=jax.ShapeDtypeStruct((n_snap, snaps_dev, comps, rows, cells_z), jnp.bfloat16),
    )(velocity, *halos)


def all_to_all_sum(x, axis):
    got = lax.all_to_all(x, axis, split_axis=0, concat_axis=0, tiled=True)
    return jnp.sum(got, axis=0)


def exchange(parts):
    arranged = lax.all_to_all(parts, "snap", split_axis=0, concat_axis=0, tiled=True)
    count, snaps_dev, comps, rows, cells_z = arranged.shape
    return arranged.reshape(count * snaps_dev, comps * rows, cells_z)


def fluctuation_of(columns, onehot, bin_counts):
    bin_sums = jnp.einsum(
        "bs,skz->bkz", onehot.astype(jnp.bfloat16), columns, preferred_element_type=jnp.float32
    )
    bin_means = bin_sums / bin_counts[:, None, None]
    high = lax.reduce_precision(bin_means, exponent_bits=8, mantissa_bits=7)
    rest = bin_means - high
    middle = lax.reduce_precision(rest, exponent_bits=8, mantissa_bits=7)
    split = jnp.concatenate([high, middle, rest - middle], axis=0).astype(jnp.bfloat16)
    selected = jnp.einsum(
        "sb,bkz->skz",
        jnp.tile(onehot.T.astype(jnp.bfloat16), (1, 3)),
        split,
        preferred_element_type=jnp.float32,
    )
    fluct = (columns.astype(jnp.float32) - selected).astype(jnp.bfloat16)
    return jnp.einsum("skz,tkz->st", fluct, fluct, preferred_element_type=jnp.float32)


def body(velocity, phase_bins, tile_owner):
    _, _, cells_x, cells_y, cells_z = velocity.shape
    n_snap = lax.axis_size("snap")
    count = lax.axis_size("space")
    forward = [(i, i + 1) for i in range(count - 1)]
    backward = [(target, source) for source, target in forward]
    low = lax.ppermute(velocity[:, 1:3, cells_x - 2 :], "space", forward)
    high = lax.ppermute(velocity[:, 1:3, :2], "space", backward)

    parts_x = curl_call(curl_x_kernel, 1, velocity, [], n_snap)
    cols_x = exchange(parts_x)
    cols_yz = exchange(curl_call(curl_yz_kernel, 2, velocity, [low, high], n_snap))
    total_snaps = cols_x.shape[0]

    onehot = (phase_bins[None, :] == jnp.arange(NB, dtype=jnp.int32)[:, None])
    bin_counts = jnp.sum(onehot.astype(jnp.float32), axis=1)
    voxel_total = lax.axis_size("space") * cells_x * cells_y * cells_z
    partial_gram = (
        fluctuation_of(cols_x, onehot, bin_counts) + fluctuation_of(cols_yz, onehot, bin_counts)
    ) / voxel_total

    row_blocks = partial_gram.reshape(n_snap, total_snaps // n_snap, total_snaps)
    col_sum = all_to_all_sum(row_blocks, "snap")
    tile_count = lax.axis_size("space")
    tile_ids = jnp.arange(tile_count, dtype=jnp.int32)
    owned = (tile_owner[None, :] == tile_ids[:, None]).astype(jnp.float32)
    tiles = col_sum.reshape(col_sum.shape[0], tile_count, total_snaps // tile_count)
    tiles = jnp.einsum(
        "kt,atr->kra", owned, tiles, precision=lax.Precision.HIGHEST, preferred_element_type=jnp.float32
    )
    lanes = 128
    mine = all_to_all_sum(tiles.reshape(tile_count, -1, lanes), "space")
    return mine.reshape(1, total_snaps // tile_count, -1)


def solution(mesh):
    return jax.shard_map(
        body,
        mesh=mesh,
        in_specs=(P("snap", None, "space", None, None), P(), P()),
        out_specs=P("space", None, "snap"),
        check_vma=False,
    )
```
